32 devices in a mesh: mol: 2 (over x), occ: 16 (over z, y, core).
Axes of the slice: x: 2, y: 2, z: 4, core: 2. Of those that a mesh axis runs over, the one named last changes fastest.
Arguments:
- integrals: bfloat16 [512, 128, 2048], P(('mol', 'occ')), parts along dimension 0, may hold values from -6 to 6
- orbitals: bfloat16 [4096, 1536], P('mol'), parts along dimension 0
- occ_energy: float32 [256], P('mol'), parts along dimension 0, may hold values from -2 to -0.3
- vir_energy: float32 [3072], P('mol'), parts along dimension 0, may hold values from 0.1 to 3
- owner: int32 [16], P('mol'), parts along dimension 0, may hold values from 0 to 127
- vblock: int32 [16], P('mol'), parts along dimension 0, may hold values from 0 to 7
Outputs:
- factors: bfloat16 [512, 128, 1536], P('mol', 'occ'), parts along dimension 0
- pair_energy: float32 [256, 8], P(('mol', 'occ')), parts along dimension 0
The draws below stay inside these ranges and needn't reach their ends.
There are 2 independent parts, one for each index of `mol`. The reference program is written for one: setup_inputs(seed, part) draws one part's arguments, and reference() takes and returns one part's arrays. A program takes and returns all parts, laid end to end along the dimension named above; each array names one. Nothing has to cross between parts.
Inputs may be any that keep to these rules, and one draw needn't show every extreme that they name: `owner`: each step names one occupied orbital and one virtual block; steps may repeat.
All inputs are finite; a program needn't handle non-finite values.
Results may differ from the reference program's by a relative error of at most 0.001.
Values may be sent and summed in bfloat16 or wider, within the bound.
No kernel may reach another device: no remote copies, remote signals or barrier semaphores. Data moves between devices by JAX's collectives and lax.ppermute only.
A program may use at most 128 MiB of HBM per device.

```python
import jax
import jax.numpy as jnp
from jax import lax

NBASIS = 2048
NVIR = 1536
NOCC = 128
NAUX = 256
VBLK = 192
STEPS = 8
NVB = 8


def draw_orbitals(key, part):
    key_scale = jax.random.fold_in(key, 11)
    key_entry = jax.random.fold_in(key, 12)
    logs = jax.random.uniform(key_scale, (NVIR,), jnp.float32, jnp.log(0.3), jnp.log(3.0))
    entries = jax.random.normal(key_entry, (NBASIS, NVIR), jnp.float32)
    values = entries * jnp.exp(logs)[None, :] / jnp.sqrt(jnp.float32(NBASIS))
    return values.astype(jnp.bfloat16)


def place_ends(drawn, stream_key, smallest, largest):
    longest = drawn.shape.index(max(drawn.shape))
    spots = []
    for shift in (0, 1):
        where = [jax.random.randint(jax.random.fold_in(stream_key, axis), (), 0, length) for axis, length in enumerate(drawn.shape)]
        where[longest] = (where[longest] + shift) % drawn.shape[longest]
        spots.append(tuple(where))
    return drawn.at[spots[0]].set(smallest).at[spots[1]].set(largest)


def block_levels(stream_key, shape, shards, low, largest):
    def one(dim, shards_of):
        heights = jax.random.uniform(jax.random.fold_in(jax.random.fold_in(stream_key, 6), dim), (shards_of,), jnp.float32, low / len(shards), largest / len(shards))
        return jnp.repeat(jnp.exp(heights), shape[dim] // shards_of).reshape((-1,) + (1,) * (len(shape) - dim - 1))

    loudness = one(*shards[0])
    for cut in shards[1:]:
        loudness = loudness * one(*cut)
    return loudness


def normal_values(rng, shape, deviation, most, split=(), held_as=jnp.bfloat16):
    values = jax.random.normal(rng, shape, jnp.float32) * deviation
    if len(split) > 0:
        values = block_levels(rng, shape, split, -0.22, 0.18) * values
    return jnp.clip(values, min=-most, max=most).astype(held_as)


def setup_inputs(seed: int = 0, part: int = 0) -> dict:
    streams_of = jax.random.split(jax.random.key(seed), 7)
    part_splits = jax.random.split(jax.random.fold_in(streams_of[6], part), 7)
    integrals = normal_values(part_splits[0], (NAUX, NOCC, NBASIS), 1.0, 6.0, ((0, 16),))
    orbitals = draw_orbitals(jax.random.fold_in(jax.random.fold_in(streams_of[6], part), 71), part)
    occ_energy = jnp.clip(jax.random.uniform(part_splits[2], (NOCC,), jnp.float32, -2.0, -0.3), -2.0, -0.3)
    vir_energy = jnp.clip(jax.random.uniform(part_splits[3], (NVIR,), jnp.float32, 0.1, 3.0), 0.1, 3.0)
    owner = place_ends(jax.random.randint(part_splits[4], (STEPS,), 0, NOCC), jax.random.fold_in(part_splits[4], 1), 0, NOCC - 1).astype(jnp.int32)
    vblock = place_ends(jax.random.randint(part_splits[5], (STEPS,), 0, NVB), jax.random.fold_in(part_splits[5], 1), 0, NVB - 1).astype(jnp.int32)
    return dict(integrals=integrals, orbitals=orbitals, occ_energy=occ_energy, vir_energy=vir_energy, owner=owner, vblock=vblock)


def reference(integrals, orbitals, occ_energy, vir_energy, owner, vblock):
    flat = integrals.reshape(NAUX * NOCC, NBASIS)
    factors = jnp.dot(flat, orbitals, preferred_element_type=jnp.float32).astype(jnp.bfloat16).reshape(NAUX, NOCC, NVIR)
    wide = factors.astype(jnp.float32)
    scale = 1.0 / (NAUX * NVIR * VBLK)

    def one_step(pair):
        orbital_j, block_id = pair
        start = (block_id * VBLK).astype(jnp.int32)
        block = lax.dynamic_slice(wide, (jnp.int32(0), orbital_j.astype(jnp.int32), start), (NAUX, 1, VBLK))[:, 0, :]
        coulomb = lax.dot_general(wide, block, (((0,), (0,)), ((), ())))
        vir_block = lax.dynamic_slice(vir_energy, (start,), (VBLK,))
        occ_j = occ_energy[orbital_j]
        denom = vir_energy[None, :, None] + vir_block[None, None, :] - occ_energy[:, None, None] - occ_j
        return -jnp.sum(coulomb * coulomb / denom, axis=(1, 2)) * scale

    energies = lax.map(one_step, (owner, vblock))
    return factors, jnp.transpose(energies).astype(jnp.float32)
```

```python
import jax
import jax.numpy as jnp
from jax import lax
from jax.sharding import PartitionSpec as P

VBLK = 192


def pair_column(factors, block, occ_here, occ_energy, vir_energy, orbital_j, block_id):
    coulomb = lax.dot_general(
        factors, block, (((0,), (0,)), ((), ())), preferred_element_type=jnp.float32
    )
    vir_block = lax.dynamic_slice(vir_energy, (block_id * VBLK,), (VBLK,))
    occ_j = occ_energy[orbital_j]
    denom = vir_energy[None, :, None] + vir_block[None, None, :] - occ_here[:, None, None] - occ_j
    scale = 1.0 / (factors.shape[0] * vir_energy.shape[0] * VBLK)
    return -jnp.sum(coulomb * coulomb / denom, axis=(1, 2)) * scale


def per_device(integrals, orbitals, occ_energy, vir_energy, owner, vblock):
    aux_here, occ_total, basis_count = integrals.shape
    step_count = owner.shape[0]
    flat = integrals.reshape(aux_here * occ_total, basis_count)
    product = jnp.dot(flat, orbitals, preferred_element_type=jnp.float32).astype(jnp.bfloat16)
    product = product.reshape(aux_here, occ_total, orbitals.shape[1])

    def own_piece(step):
        piece = lax.dynamic_slice(
            product, (jnp.int32(0), owner[step], vblock[step] * VBLK), (aux_here, 1, VBLK)
        )
        return piece[:, 0, :]

    pieces = jnp.stack([own_piece(step) for step in range(step_count)], axis=1)
    blocks = lax.all_gather(pieces, "occ", axis=0, tiled=True)
    factors = lax.all_to_all(product, "occ", split_axis=1, concat_axis=0, tiled=True)
    local_count = factors.shape[1]
    occ_here = lax.dynamic_slice(occ_energy, (lax.axis_index("occ") * local_count,), (local_count,))
    energies = jnp.zeros((local_count, step_count), jnp.float32)

    def step_body(step, energies):
        orbital_j = owner[step]
        block_id = vblock[step]
        block = lax.dynamic_index_in_dim(blocks, step, axis=1, keepdims=False)
        column = pair_column(factors, block, occ_here, occ_energy, vir_energy, orbital_j, block_id)
        return lax.dynamic_update_slice(energies, column[:, None], (jnp.int32(0), step))

    energies = lax.fori_loop(0, step_count, step_body, energies)
    return (factors, energies)


def solution(mesh):
    placed = (P(("mol", "occ"), None, None), P("mol", None), P("mol"), P("mol"), P("mol"), P("mol"))
    return jax.shard_map(
        per_device,
        mesh=mesh,
        in_specs=placed,
        out_specs=(P("mol", "occ", None), P(("mol", "occ"), None)),
        check_vma=False,
    )
```

```python
import jax
import jax.numpy as jnp
from jax import lax
from jax.sharding import PartitionSpec as P

VBLK = 192
CHUNKS = 4


def chunk_energies(factors, blocks, occ_rows, occ_cols, vir_energy, vir_blocks, scale):
    coulomb = lax.dot_general(
        factors, blocks, (((0,), (0,)), ((), ())), preferred_element_type=jnp.float32
    )
    denom = (
        vir_energy[None, :, None, None]
        + vir_blocks[None, None, :, :]
        - occ_rows[:, None, None, None]
        - occ_cols[None, None, :, None]
    )
    return -jnp.sum(coulomb * coulomb / denom, axis=(1, 3)) * scale


def per_device(integrals, orbitals, occ_energy, vir_energy, owner, vblock):
    aux_here, occ_total, basis_count = integrals.shape
    nvir = orbitals.shape[1]
    step_count = owner.shape[0]
    groups = lax.psum(1, "occ")
    local_count = occ_total // groups
    chunks = CHUNKS
    while local_count % chunks:
        chunks -= 1
    width = local_count // chunks
    flat = integrals.reshape(aux_here * occ_total, basis_count)
    product = jnp.dot(flat, orbitals, preferred_element_type=jnp.float32).astype(jnp.bfloat16)
    product = product.reshape(aux_here, groups, local_count, nvir)

    def own_piece(step):
        piece = lax.dynamic_slice(
            product.reshape(aux_here, occ_total, nvir),
            (jnp.int32(0), owner[step], vblock[step] * VBLK),
            (aux_here, 1, VBLK),
        )
        return piece[:, 0, :]

    pieces = jnp.stack([own_piece(step) for step in range(step_count)], axis=1)
    pieces = pieces.reshape(aux_here, 1, 1, step_count * VBLK)
    extra = jnp.broadcast_to(pieces, (aux_here, groups, 1, step_count * VBLK))

    me = lax.axis_index("occ")
    occ_here = lax.dynamic_slice(occ_energy, (me * local_count,), (local_count,))
    occ_cols = occ_energy[owner]
    vir_blocks = jnp.stack(
        [lax.dynamic_slice(vir_energy, (vblock[s] * VBLK,), (VBLK,)) for s in range(step_count)]
    )
    scale = 1.0 / (aux_here * groups * nvir * VBLK)

    parts = []
    columns = []
    blocks = None
    for c in range(chunks):
        payload = product[:, :, c * width:(c + 1) * width, :]
        if c == 0 and step_count * VBLK == nvir:
            payload = jnp.concatenate([payload, extra], axis=2)
        payload = payload.reshape(aux_here, groups * payload.shape[2], nvir)
        if c >= 1:
            held = (parts[-1],) + tuple(columns[-2:-1])
            payload, _ = lax.optimization_barrier((payload, held))
        got = lax.all_to_all(payload, "occ", split_axis=1, concat_axis=0, tiled=True)
        if c == 0:
            if step_count * VBLK == nvir:
                blocks = got[:, width, :].reshape(aux_here * groups, step_count, VBLK)
                got = got[:, :width, :]
            else:
                blocks = lax.all_gather(
                    pieces.reshape(aux_here, step_count, VBLK), "occ", axis=0, tiled=True
                )
        parts.append(got)
        columns.append(
            chunk_energies(
                got, blocks, occ_here[c * width:(c + 1) * width], occ_cols,
                vir_energy, vir_blocks, scale,
            )
        )
    factors = jnp.concatenate(parts, axis=1)
    energies = jnp.concatenate(columns, axis=0)
    return (factors, energies)


def solution(mesh):
    placed = (P(("mol", "occ"), None, None), P("mol", None), P("mol"), P("mol"), P("mol"), P("mol"))
    return jax.shard_map(
        per_device,
        mesh=mesh,
        in_specs=placed,
        out_specs=(P("mol", "occ", None), P(("mol", "occ"), None)),
        check_vma=False,
    )
```

```python
import jax
import jax.numpy as jnp
from jax import lax
from jax.sharding import PartitionSpec as P

VBLK = 192
CHUNKS = 4


def chunk_energies(factors, blocks, occ_rows, occ_cols, vir_chunk, vir_blocks, scale):
    coulomb = lax.dot_general(
        factors, blocks, (((0,), (0,)), ((), ())), preferred_element_type=jnp.float32
    )
    denom = (
        vir_chunk[None, :, None, None]
        + vir_blocks[None, None, :, :]
        - occ_rows[:, None, None, None]
        - occ_cols[None, None, :, None]
    )
    return jnp.sum(coulomb * coulomb / denom, axis=(1, 3))


def per_device(integrals, orbitals, occ_energy, vir_energy, owner, vblock):
    aux_here, occ_total, basis_count = integrals.shape
    nvir = orbitals.shape[1]
    step_count = owner.shape[0]
    groups = lax.psum(1, "occ")
    local_count = occ_total // groups
    chunks = CHUNKS
    while nvir % (chunks * 128):
        chunks -= 1
    span = nvir // chunks
    ride = step_count == local_count
    rows = integrals.reshape(aux_here, groups, local_count, basis_count)
    rows = jnp.transpose(rows, (1, 0, 2, 3))

    picked = jnp.take(integrals, owner, axis=1)
    picked = jnp.dot(
        picked.reshape(aux_here * step_count, basis_count), orbitals,
        preferred_element_type=jnp.float32,
    ).astype(jnp.bfloat16).reshape(aux_here, step_count, nvir)
    pieces = jnp.stack(
        [lax.dynamic_slice_in_dim(picked[:, s, :], vblock[s] * VBLK, VBLK, axis=1) for s in range(step_count)],
        axis=1,
    )

    me = lax.axis_index("occ")
    occ_here = lax.dynamic_slice(occ_energy, (me * local_count,), (local_count,))
    occ_cols = occ_energy[owner]
    vir_blocks = jnp.stack(
        [lax.dynamic_slice(vir_energy, (vblock[s] * VBLK,), (VBLK,)) for s in range(step_count)]
    )
    scale = 1.0 / (aux_here * groups * nvir * VBLK)

    if not ride:
        blocks = lax.all_gather(pieces, "occ", axis=0, tiled=True)
    parts = []
    sums = []
    factors = jnp.zeros((groups * aux_here, local_count, nvir), jnp.bfloat16)
    for c in range(chunks):
        cols = slice(c * span, (c + 1) * span)
        product = lax.dot_general(
            rows, orbitals[:, cols], (((3,), (0,)), ((), ())),
            preferred_element_type=jnp.float32,
        ).astype(jnp.bfloat16)
        if c == 0 and ride:
            extra = jnp.broadcast_to(pieces[None], (groups, aux_here, step_count, VBLK))
            product = jnp.concatenate([product, extra], axis=3)
        if c >= 1:
            held = (parts[-1],) + tuple(sums[-2:-1])
            product, _ = lax.optimization_barrier((product, held))
        got = lax.all_to_all(product, "occ", split_axis=0, concat_axis=0, tiled=True)
        got = got.reshape(groups * aux_here, local_count, got.shape[-1])
        if c == 0 and ride:
            blocks = got[:, :, span:]
            got = got[:, :, :span]
        parts.append(got)
        factors = lax.dynamic_update_slice(factors, got, (0, 0, c * span))
        sums.append(
            chunk_energies(lax.optimization_barrier(got), blocks, occ_here, occ_cols, vir_energy[cols], vir_blocks, scale)
        )
    total = sums[0]
    for extra_sum in sums[1:]:
        total = total + extra_sum
    energies = -total * scale
    return (factors, energies)


def solution(mesh):
    placed = (P(("mol", "occ"), None, None), P("mol", None), P("mol"), P("mol"), P("mol"), P("mol"))
    return jax.shard_map(
        per_device,
        mesh=mesh,
        in_specs=placed,
        out_specs=(P("mol", "occ", None), P(("mol", "occ"), None)),
        check_vma=False,
    )
```

```python
import jax
import jax.numpy as jnp
from jax import lax
from jax.sharding import PartitionSpec as P

VBLK = 192
TAIL_PART = 4


def chunk_energies(factors, blocks, occ_rows, occ_cols, vir_chunk, vir_blocks, scale):
    coulomb = lax.dot_general(
        factors, blocks, (((0,), (0,)), ((), ())), preferred_element_type=jnp.float32
    )
    denom = (
        vir_chunk[None, :, None, None]
        + vir_blocks[None, None, :, :]
        - occ_rows[:, None, None, None]
        - occ_cols[None, None, :, None]
    )
    return jnp.sum(coulomb * coulomb / denom, axis=(1, 3))


def per_device(integrals, orbitals, occ_energy, vir_energy, owner, vblock):
    aux_here, occ_total, basis_count = integrals.shape
    nvir = orbitals.shape[1]
    step_count = owner.shape[0]
    groups = lax.psum(1, "occ")
    local_count = occ_total // groups
    if nvir % 128 == 0 and nvir >= 256:
        tail = max(1, (nvir // 128) // TAIL_PART) * 128
        bounds = [0, nvir - tail, nvir]
    else:
        bounds = [0, nvir]
    chunks = len(bounds) - 1
    ride = step_count == local_count
    rows = integrals.reshape(aux_here, groups, local_count, basis_count)
    rows = jnp.transpose(rows, (1, 0, 2, 3))

    picked = jnp.take(integrals, owner, axis=1)
    picked = jnp.dot(
        picked.reshape(aux_here * step_count, basis_count), orbitals,
        preferred_element_type=jnp.float32,
    ).astype(jnp.bfloat16).reshape(aux_here, step_count, nvir)
    pieces = jnp.stack(
        [lax.dynamic_slice_in_dim(picked[:, s, :], vblock[s] * VBLK, VBLK, axis=1) for s in range(step_count)],
        axis=1,
    )

    me = lax.axis_index("occ")
    occ_here = lax.dynamic_slice(occ_energy, (me * local_count,), (local_count,))
    occ_cols = occ_energy[owner]
    vir_blocks = jnp.stack(
        [lax.dynamic_slice(vir_energy, (vblock[s] * VBLK,), (VBLK,)) for s in range(step_count)]
    )
    scale = 1.0 / (aux_here * groups * nvir * VBLK)

    if not ride:
        blocks = lax.all_gather(pieces, "occ", axis=0, tiled=True)
    parts = []
    sums = []
    for c in range(chunks):
        cols = slice(bounds[c], bounds[c + 1])
        span = bounds[c + 1] - bounds[c]
        product = lax.dot_general(
            rows, orbitals[:, cols], (((3,), (0,)), ((), ())),
            preferred_element_type=jnp.float32,
        ).astype(jnp.bfloat16)
        if c == 0 and ride:
            extra = jnp.broadcast_to(pieces[None], (groups, aux_here, step_count, VBLK))
            product = jnp.concatenate([product, extra], axis=3)
        if c >= 1:
            held = (parts[-1],) + tuple(sums[-2:-1])
            product, _ = lax.optimization_barrier((product, held))
        got = lax.all_to_all(product, "occ", split_axis=0, concat_axis=0, tiled=True)
        got = got.reshape(groups * aux_here, local_count, got.shape[-1])
        if c == 0 and ride:
            blocks = got[:, :, span:]
            got = got[:, :, :span]
        parts.append(got)
        if c == 0:
            factors = jnp.pad(got, ((0, 0), (0, 0), (0, nvir - span)))
        else:
            factors = lax.dynamic_update_slice(factors, got, (0, 0, bounds[c]))
        sums.append(
            chunk_energies(
                lax.optimization_barrier(got), blocks, occ_here, occ_cols,
                vir_energy[cols], vir_blocks, scale,
            )
        )
        if c == 0:
            factors, sums[0] = lax.optimization_barrier((factors, sums[0]))
    total = sums[0]
    for extra_sum in sums[1:]:
        total = total + extra_sum
    energies = -total * scale
    return (factors, energies)


def solution(mesh):
    placed = (P(("mol", "occ"), None, None), P("mol", None), P("mol"), P("mol"), P("mol"), P("mol"))
    return jax.shard_map(
        per_device,
        mesh=mesh,
        in_specs=placed,
        out_specs=(P("mol", "occ", None), P(("mol", "occ"), None)),
        check_vma=False,
    )
```

```python
import jax
import jax.numpy as jnp
from jax import lax
from jax.sharding import PartitionSpec as P

VBLK = 192
TAIL_PART = 0


def chunk_energies(factors, blocks, occ_rows, occ_cols, vir_chunk, vir_blocks, scale):
    coulomb = lax.dot_general(
        factors, blocks, (((0,), (0,)), ((), ())), preferred_element_type=jnp.float32
    )
    denom = (
        vir_chunk[None, :, None, None]
        + vir_blocks[None, None, :, :]
        - occ_rows[:, None, None, None]
        - occ_cols[None, None, :, None]
    )
    return jnp.sum(coulomb * coulomb / denom, axis=(1, 3))


def per_device(integrals, orbitals, occ_energy, vir_energy, owner, vblock):
    aux_here, occ_total, basis_count = integrals.shape
    nvir = orbitals.shape[1]
    step_count = owner.shape[0]
    groups = lax.psum(1, "occ")
    local_count = occ_total // groups
    if TAIL_PART and nvir % 128 == 0 and nvir >= 256:
        tail = max(1, (nvir // 128) // TAIL_PART) * 128
        bounds = [0, nvir - tail, nvir]
    else:
        bounds = [0, nvir]
    chunks = len(bounds) - 1
    ride = step_count == local_count
    rows = integrals.reshape(aux_here, groups, local_count, basis_count)
    rows = jnp.transpose(rows, (1, 0, 2, 3))

    picked = jnp.take(integrals, owner, axis=1)
    picked = jnp.dot(
        picked.reshape(aux_here * step_count, basis_count), orbitals,
        preferred_element_type=jnp.float32,
    ).astype(jnp.bfloat16).reshape(aux_here, step_count, nvir)
    pieces = jnp.stack(
        [lax.dynamic_slice_in_dim(picked[:, s, :], vblock[s] * VBLK, VBLK, axis=1) for s in range(step_count)],
        axis=1,
    )

    me = lax.axis_index("occ")
    occ_here = lax.dynamic_slice(occ_energy, (me * local_count,), (local_count,))
    occ_cols = occ_energy[owner]
    vir_blocks = jnp.stack(
        [lax.dynamic_slice(vir_energy, (vblock[s] * VBLK,), (VBLK,)) for s in range(step_count)]
    )
    scale = 1.0 / (aux_here * groups * nvir * VBLK)

    if not ride:
        blocks = lax.all_gather(pieces, "occ", axis=0, tiled=True)
    parts = []
    sums = []
    for c in range(chunks):
        cols = slice(bounds[c], bounds[c + 1])
        span = bounds[c + 1] - bounds[c]
        product = lax.dot_general(
            rows, orbitals[:, cols], (((3,), (0,)), ((), ())),
            preferred_element_type=jnp.float32,
        ).astype(jnp.bfloat16)
        if c == 0 and ride:
            extra = jnp.broadcast_to(pieces[None], (groups, aux_here, step_count, VBLK))
            product = jnp.concatenate([product, extra], axis=3)
        if c >= 1:
            held = (parts[-1],) + tuple(sums[-2:-1])
            product, _ = lax.optimization_barrier((product, held))
        got = lax.all_to_all(product, "occ", split_axis=0, concat_axis=0, tiled=True)
        got = got.reshape(groups * aux_here, local_count, got.shape[-1])
        if c == 0 and ride:
            blocks = got[:, :, span:]
            got = got[:, :, :span]
        parts.append(got)
        if c == 0:
            factors = jnp.pad(got, ((0, 0), (0, 0), (0, nvir - span)))
        else:
            factors = lax.dynamic_update_slice(factors, got, (0, 0, bounds[c]))
        sums.append(
            chunk_energies(
                lax.optimization_barrier(got), blocks, occ_here, occ_cols,
                vir_energy[cols], vir_blocks, scale,
            )
        )
        if c == 0:
            factors, sums[0] = lax.optimization_barrier((factors, sums[0]))
    total = sums[0]
    for extra_sum in sums[1:]:
        total = total + extra_sum
    energies = -total * scale
    return (factors, energies)


def solution(mesh):
    placed = (P(("mol", "occ"), None, None), P("mol", None), P("mol"), P("mol"), P("mol"), P("mol"))
    return jax.shard_map(
        per_device,
        mesh=mesh,
        in_specs=placed,
        out_specs=(P("mol", "occ", None), P(("mol", "occ"), None)),
        check_vma=False,
    )
```

```python
import jax
import jax.numpy as jnp
from jax import lax
from jax.sharding import PartitionSpec as P

VBLK = 192
TAIL_PART = 4


def chunk_energies(factors, blocks, occ_rows, occ_cols, vir_chunk, vir_blocks, scale):
    coulomb = lax.dot_general(
        factors, blocks, (((0,), (0,)), ((), ())), preferred_element_type=jnp.float32
    )
    denom = (
        vir_chunk[None, :, None, None]
        + vir_blocks[None, None, :, :]
        - occ_rows[:, None, None, None]
        - occ_cols[None, None, :, None]
    )
    return jnp.sum(coulomb * coulomb / denom, axis=(1, 3))


def per_device(integrals, orbitals, occ_energy, vir_energy, owner, vblock):
    aux_here, occ_total, basis_count = integrals.shape
    nvir = orbitals.shape[1]
    step_count = owner.shape[0]
    groups = lax.psum(1, "occ")
    local_count = occ_total // groups
    if nvir % 128 == 0 and nvir >= 256:
        tail = max(1, (nvir // 128) // TAIL_PART) * 128
        bounds = [0, nvir - tail, nvir]
    else:
        bounds = [0, nvir]
    chunks = len(bounds) - 1
    ride = step_count == local_count
    rows = integrals.reshape(aux_here, groups, local_count, basis_count)
    rows = jnp.transpose(rows, (1, 0, 2, 3))

    picked = jnp.take(integrals, owner, axis=1)
    picked = jnp.dot(
        picked.reshape(aux_here * step_count, basis_count), orbitals,
        preferred_element_type=jnp.float32,
    ).astype(jnp.bfloat16).reshape(aux_here, step_count, nvir)
    pieces = jnp.stack(
        [lax.dynamic_slice_in_dim(picked[:, s, :], vblock[s] * VBLK, VBLK, axis=1) for s in range(step_count)],
        axis=1,
    )

    me = lax.axis_index("occ")
    occ_here = lax.dynamic_slice(occ_energy, (me * local_count,), (local_count,))
    occ_cols = occ_energy[owner]
    vir_blocks = jnp.stack(
        [lax.dynamic_slice(vir_energy, (vblock[s] * VBLK,), (VBLK,)) for s in range(step_count)]
    )
    scale = 1.0 / (aux_here * groups * nvir * VBLK)

    if not ride:
        blocks = lax.all_gather(pieces, "occ", axis=0, tiled=True)
    parts = []
    raw = []
    sums = []
    for c in range(chunks):
        cols = slice(bounds[c], bounds[c + 1])
        span = bounds[c + 1] - bounds[c]
        product = lax.dot_general(
            rows, orbitals[:, cols], (((3,), (0,)), ((), ())),
            preferred_element_type=jnp.float32,
        ).astype(jnp.bfloat16)
        if c == 0 and ride:
            extra = jnp.broadcast_to(pieces[None], (groups, aux_here, step_count, VBLK))
            product = jnp.concatenate([product, extra], axis=3)
        if c >= 1:
            held = (raw[-1],) + tuple(sums[-2:-1])
            product, _ = lax.optimization_barrier((product, held))
        got = lax.all_to_all(product, "occ", split_axis=0, concat_axis=0, tiled=True)
        raw.append(got)
        got = got.reshape(groups * aux_here, local_count, got.shape[-1])
        if c == 0 and ride:
            blocks = got[:, :, span:]
            got = got[:, :, :span]
        parts.append(got)
        if c == 0:
            factors = jnp.pad(got, ((0, 0), (0, 0), (0, nvir - span)))
        else:
            factors = lax.dynamic_update_slice(factors, got, (0, 0, bounds[c]))
        if c == 0 and ride:
            whole = raw[-1].reshape(groups * aux_here, local_count, span + VBLK)
            vir_here = jnp.concatenate(
                [vir_energy[cols], jnp.full((VBLK,), jnp.inf, vir_energy.dtype)]
            )
        else:
            whole = lax.optimization_barrier(got)
            vir_here = vir_energy[cols]
        sums.append(
            chunk_energies(whole, blocks, occ_here, occ_cols, vir_here, vir_blocks, scale)
        )
        if c == 0:
            factors, sums[0] = lax.optimization_barrier((factors, sums[0]))
    total = sums[0]
    for extra_sum in sums[1:]:
        total = total + extra_sum
    energies = -total * scale
    return (factors, energies)


def solution(mesh):
    placed = (P(("mol", "occ"), None, None), P("mol", None), P("mol"), P("mol"), P("mol"), P("mol"))
    return jax.shard_map(
        per_device,
        mesh=mesh,
        in_specs=placed,
        out_specs=(P("mol", "occ", None), P(("mol", "occ"), None)),
        check_vma=False,
    )
```

```python
import jax
import jax.numpy as jnp
from jax import lax
from jax.sharding import PartitionSpec as P

VBLK = 192
EDGE_PART = 4


def chunk_energies(factors, blocks, occ_rows, occ_cols, vir_chunk, vir_blocks, scale):
    coulomb = lax.dot_general(
        factors, blocks, (((0,), (0,)), ((), ())), preferred_element_type=jnp.float32
    )
    denom = (
        vir_chunk[None, :, None, None]
        + vir_blocks[None, None, :, :]
        - occ_rows[:, None, None, None]
        - occ_cols[None, None, :, None]
    )
    return jnp.sum(coulomb * coulomb / denom, axis=(1, 3))


def per_device(integrals, orbitals, occ_energy, vir_energy, owner, vblock):
    aux_here, occ_total, basis_count = integrals.shape
    nvir = orbitals.shape[1]
    step_count = owner.shape[0]
    groups = lax.psum(1, "occ")
    local_count = occ_total // groups
    tiles = nvir // 128 if nvir % 128 == 0 else 0
    edge = tiles // EDGE_PART
    if edge >= 1 and tiles - 2 * edge >= 1:
        bounds = [0, edge * 128, nvir - edge * 128, nvir]
    else:
        bounds = [0, nvir]
    chunks = len(bounds) - 1
    ride = step_count == local_count
    rows = integrals.reshape(aux_here, groups, local_count, basis_count)
    rows = jnp.transpose(rows, (1, 0, 2, 3))

    def chunk_product(c):
        return lax.dot_general(
            rows, orbitals[:, bounds[c]:bounds[c + 1]], (((3,), (0,)), ((), ())),
            preferred_element_type=jnp.float32,
        ).astype(jnp.bfloat16)

    first_product = chunk_product(0)
    first_product, late = lax.optimization_barrier((first_product, owner))
    picked = jnp.take(integrals, late, axis=1)
    picked = jnp.dot(
        picked.reshape(aux_here * step_count, basis_count), orbitals,
        preferred_element_type=jnp.float32,
    ).astype(jnp.bfloat16).reshape(aux_here, step_count, nvir)
    pieces = jnp.stack(
        [lax.dynamic_slice_in_dim(picked[:, s, :], vblock[s] * VBLK, VBLK, axis=1) for s in range(step_count)],
        axis=1,
    )

    me = lax.axis_index("occ")
    occ_here = lax.dynamic_slice(occ_energy, (me * local_count,), (local_count,))
    occ_cols = occ_energy[owner]
    vir_blocks = jnp.stack(
        [lax.dynamic_slice(vir_energy, (vblock[s] * VBLK,), (VBLK,)) for s in range(step_count)]
    )
    scale = 1.0 / (aux_here * groups * nvir * VBLK)

    if not ride:
        blocks = lax.all_gather(pieces, "occ", axis=0, tiled=True)
    parts = []
    raw = []
    sums = []
    for c in range(chunks):
        cols = slice(bounds[c], bounds[c + 1])
        span = bounds[c + 1] - bounds[c]
        product = first_product if c == 0 else chunk_product(c)
        if c == 0 and ride:
            extra = jnp.broadcast_to(pieces[None], (groups, aux_here, step_count, VBLK))
            product = jnp.concatenate([product, extra], axis=3)
        if c >= 1:
            held = (raw[-1],) + tuple(sums[-2:-1])
            product, _ = lax.optimization_barrier((product, held))
        got = lax.all_to_all(product, "occ", split_axis=0, concat_axis=0, tiled=True)
        raw.append(got)
        got = got.reshape(groups * aux_here, local_count, got.shape[-1])
        if c == 0 and ride:
            blocks = got[:, :, span:]
            got = got[:, :, :span]
        parts.append(got)
        if c == 0:
            factors = jnp.pad(got, ((0, 0), (0, 0), (0, nvir - span)))
        else:
            factors = lax.dynamic_update_slice(factors, got, (0, 0, bounds[c]))
        if c == 0 and ride:
            whole = raw[-1].reshape(groups * aux_here, local_count, span + VBLK)
            vir_here = jnp.concatenate(
                [vir_energy[cols], jnp.full((VBLK,), jnp.inf, vir_energy.dtype)]
            )
        else:
            whole = lax.optimization_barrier(got)
            vir_here = vir_energy[cols]
        sums.append(
            chunk_energies(whole, blocks, occ_here, occ_cols, vir_here, vir_blocks, scale)
        )
        if c == 0:
            factors, sums[0] = lax.optimization_barrier((factors, sums[0]))
    total = sums[0]
    for extra_sum in sums[1:]:
        total = total + extra_sum
    energies = -total * scale
    return (factors, energies)


def solution(mesh):
    placed = (P(("mol", "occ"), None, None), P("mol", None), P("mol"), P("mol"), P("mol"), P("mol"))
    return jax.shard_map(
        per_device,
        mesh=mesh,
        in_specs=placed,
        out_specs=(P("mol", "occ", None), P(("mol", "occ"), None)),
        check_vma=False,
    )
```

```python
import jax
import jax.numpy as jnp
from jax import lax
from jax.sharding import PartitionSpec as P

VBLK = 192
EDGE_PART = 4


def chunk_energies(factors, blocks, occ_rows, occ_cols, vir_chunk, vir_blocks, scale):
    coulomb = lax.dot_general(
        factors, blocks, (((0,), (0,)), ((), ())), preferred_element_type=jnp.float32
    )
    denom = (
        vir_chunk[None, :, None, None]
        + vir_blocks[None, None, :, :]
        - occ_rows[:, None, None, None]
        - occ_cols[None, None, :, None]
    )
    return jnp.sum(coulomb * coulomb / denom, axis=(1, 3))


def per_device(integrals, orbitals, occ_energy, vir_energy, owner, vblock):
    aux_here, occ_total, basis_count = integrals.shape
    nvir = orbitals.shape[1]
    step_count = owner.shape[0]
    groups = lax.psum(1, "occ")
    local_count = occ_total // groups
    tiles = nvir // 128 if nvir % 128 == 0 else 0
    edge = tiles // EDGE_PART
    if edge >= 1 and tiles - 2 * edge >= 1:
        bounds = [0, edge * 128, nvir - edge * 128, nvir]
    else:
        bounds = [0, nvir]
    chunks = len(bounds) - 1
    ride = step_count == local_count
    rows = integrals.reshape(aux_here, groups, local_count, basis_count)
    rows = jnp.transpose(rows, (1, 0, 2, 3))

    def chunk_product(c):
        return lax.dot_general(
            rows, orbitals[:, bounds[c]:bounds[c + 1]], (((3,), (0,)), ((), ())),
            preferred_element_type=jnp.float32,
        ).astype(jnp.bfloat16)

    first_product = chunk_product(0)
    first_product, late = lax.optimization_barrier((first_product, owner))
    picked = jnp.concatenate(
        [lax.dynamic_slice_in_dim(integrals, late[s], 1, axis=1) for s in range(step_count)],
        axis=1,
    )
    picked = jnp.dot(
        picked.reshape(aux_here * step_count, basis_count), orbitals,
        preferred_element_type=jnp.float32,
    ).astype(jnp.bfloat16).reshape(aux_here, step_count, nvir)
    pieces = jnp.stack(
        [lax.dynamic_slice_in_dim(picked[:, s, :], vblock[s] * VBLK, VBLK, axis=1) for s in range(step_count)],
        axis=1,
    )

    me = lax.axis_index("occ")
    occ_here = lax.dynamic_slice(occ_energy, (me * local_count,), (local_count,))
    occ_cols = occ_energy[owner]
    vir_blocks = jnp.stack(
        [lax.dynamic_slice(vir_energy, (vblock[s] * VBLK,), (VBLK,)) for s in range(step_count)]
    )
    scale = 1.0 / (aux_here * groups * nvir * VBLK)

    if not ride:
        blocks = lax.all_gather(pieces, "occ", axis=0, tiled=True)
    parts = []
    raw = []
    sums = []
    for c in range(chunks):
        cols = slice(bounds[c], bounds[c + 1])
        span = bounds[c + 1] - bounds[c]
        product = first_product if c == 0 else chunk_product(c)
        if c == 0 and ride:
            extra = jnp.broadcast_to(pieces[None], (groups, aux_here, step_count, VBLK))
            product = jnp.concatenate([product, extra], axis=3)
        if c >= 1:
            held = (raw[-1],) + tuple(sums[-2:-1])
            product, _ = lax.optimization_barrier((product, held))
        got = lax.all_to_all(product, "occ", split_axis=0, concat_axis=0, tiled=True)
        raw.append(got)
        got = got.reshape(groups * aux_here, local_count, got.shape[-1])
        if c == 0 and ride:
            blocks = got[:, :, span:]
            got = got[:, :, :span]
        parts.append(got)
        if c == 0:
            factors = jnp.pad(got, ((0, 0), (0, 0), (0, nvir - span)))
        else:
            factors = lax.dynamic_update_slice(factors, got, (0, 0, bounds[c]))
        if c == 0 and ride:
            whole = raw[-1].reshape(groups * aux_here, local_count, span + VBLK)
            vir_here = jnp.concatenate(
                [vir_energy[cols], jnp.full((VBLK,), jnp.inf, vir_energy.dtype)]
            )
        else:
            whole = lax.optimization_barrier(got)
            vir_here = vir_energy[cols]
        sums.append(
            chunk_energies(whole, blocks, occ_here, occ_cols, vir_here, vir_blocks, scale)
        )
        if c == 0:
            factors, sums[0] = lax.optimization_barrier((factors, sums[0]))
    total = sums[0]
    for extra_sum in sums[1:]:
        total = total + extra_sum
    energies = -total * scale
    return (factors, energies)


def solution(mesh):
    placed = (P(("mol", "occ"), None, None), P("mol", None), P("mol"), P("mol"), P("mol"), P("mol"))
    return jax.shard_map(
        per_device,
        mesh=mesh,
        in_specs=placed,
        out_specs=(P("mol", "occ", None), P(("mol", "occ"), None)),
        check_vma=False,
    )
```

```python
import jax
import jax.numpy as jnp
from jax import lax
from jax.sharding import PartitionSpec as P

VBLK = 192
EDGE_PART = 4


def chunk_energies(factors, blocks, occ_rows, occ_cols, vir_chunk, vir_blocks, scale):
    coulomb = lax.dot_general(
        factors, blocks, (((0,), (0,)), ((), ())), preferred_element_type=jnp.float32
    )
    denom = (
        vir_chunk[None, :, None, None]
        + vir_blocks[None, None, :, :]
        - occ_rows[:, None, None, None]
        - occ_cols[None, None, :, None]
    )
    return jnp.sum(coulomb * coulomb / denom, axis=(1, 3))


def per_device(integrals, orbitals, occ_energy, vir_energy, owner, vblock):
    aux_here, occ_total, basis_count = integrals.shape
    nvir = orbitals.shape[1]
    step_count = owner.shape[0]
    groups = lax.psum(1, "occ")
    local_count = occ_total // groups
    tiles = nvir // 128 if nvir % 128 == 0 else 0
    edge = tiles // EDGE_PART
    if edge >= 1 and tiles - 2 * edge >= 1:
        bounds = [0, edge * 128, nvir - edge * 128, nvir]
    else:
        bounds = [0, nvir]
    chunks = len(bounds) - 1
    ride = step_count == local_count
    rows = integrals.reshape(aux_here, groups, local_count, basis_count)
    rows = jnp.transpose(rows, (1, 0, 2, 3))

    def chunk_product(c):
        return lax.dot_general(
            rows, orbitals[:, bounds[c]:bounds[c + 1]], (((3,), (0,)), ((), ())),
            preferred_element_type=jnp.float32,
        ).astype(jnp.bfloat16)

    first_product = chunk_product(0)
    first_product, late = lax.optimization_barrier((first_product, owner))
    picked = jnp.take(integrals, late, axis=1)
    picked = jnp.dot(
        picked.reshape(aux_here * step_count, basis_count), orbitals,
        preferred_element_type=jnp.float32,
    ).astype(jnp.bfloat16).reshape(aux_here, step_count, nvir)
    pieces = jnp.stack(
        [lax.dynamic_slice_in_dim(picked[:, s, :], vblock[s] * VBLK, VBLK, axis=1) for s in range(step_count)],
        axis=1,
    )

    me = lax.axis_index("occ")
    occ_here = lax.dynamic_slice(occ_energy, (me * local_count,), (local_count,))
    occ_cols = occ_energy[owner]
    vir_blocks = jnp.stack(
        [lax.dynamic_slice(vir_energy, (vblock[s] * VBLK,), (VBLK,)) for s in range(step_count)]
    )
    scale = 1.0 / (aux_here * groups * nvir * VBLK)

    carrier = min(1, chunks - 1) if ride else -1
    if not ride:
        blocks = lax.all_gather(pieces, "occ", axis=0, tiled=True)
    raw = []
    sums = []
    made_at = {}
    pending = []
    for c in range(chunks):
        cols = slice(bounds[c], bounds[c + 1])
        span = bounds[c + 1] - bounds[c]
        product = first_product if c == 0 else chunk_product(c)
        if c == carrier:
            extra = jnp.broadcast_to(pieces[None], (groups, aux_here, step_count, VBLK))
            product = jnp.concatenate([product, extra], axis=3)
        if c >= 1:
            held = (raw[-1],) + tuple(made_at.get(c - 2, ()))
            product, _ = lax.optimization_barrier((product, held))
        got = lax.all_to_all(product, "occ", split_axis=0, concat_axis=0, tiled=True)
        raw.append(got)
        got = got.reshape(groups * aux_here, local_count, got.shape[-1])
        if c == carrier:
            blocks = got[:, :, span:]
            got = got[:, :, :span]
        if c == 0:
            factors = jnp.pad(got, ((0, 0), (0, 0), (0, nvir - span)))
        else:
            factors = lax.dynamic_update_slice(factors, got, (0, 0, bounds[c]))
        if c == carrier:
            whole = raw[-1].reshape(groups * aux_here, local_count, span + VBLK)
            vir_here = jnp.concatenate(
                [vir_energy[cols], jnp.full((VBLK,), jnp.inf, vir_energy.dtype)]
            )
        else:
            whole = lax.optimization_barrier(got)
            vir_here = vir_energy[cols]
        pending.append((whole, vir_here))
        if c >= carrier:
            made = [
                chunk_energies(view, blocks, occ_here, occ_cols, vir_k, vir_blocks, scale)
                for view, vir_k in pending
            ]
            pending = []
            if c < chunks - 1:
                factors, made[0] = lax.optimization_barrier((factors, made[0]))
            made_at[c] = made
            sums.extend(made)
    total = sums[0]
    for extra_sum in sums[1:]:
        total = total + extra_sum
    energies = -total * scale
    return (factors, energies)


def solution(mesh):
    placed = (P(("mol", "occ"), None, None), P("mol", None), P("mol"), P("mol"), P("mol"), P("mol"))
    return jax.shard_map(
        per_device,
        mesh=mesh,
        in_specs=placed,
        out_specs=(P("mol", "occ", None), P(("mol", "occ"), None)),
        check_vma=False,
    )
```

```python
import jax
import jax.numpy as jnp
from jax import lax
from jax.sharding import PartitionSpec as P

VBLK = 192
EDGE_PART = 6


def chunk_energies(factors, blocks, occ_rows, occ_cols, vir_chunk, vir_blocks, scale):
    coulomb = lax.dot_general(
        factors, blocks, (((0,), (0,)), ((), ())), preferred_element_type=jnp.float32
    )
    denom = (
        vir_chunk[None, :, None, None]
        + vir_blocks[None, None, :, :]
        - occ_rows[:, None, None, None]
        - occ_cols[None, None, :, None]
    )
    return jnp.sum(coulomb * coulomb / denom, axis=(1, 3))


def per_device(integrals, orbitals, occ_energy, vir_energy, owner, vblock):
    aux_here, occ_total, basis_count = integrals.shape
    nvir = orbitals.shape[1]
    step_count = owner.shape[0]
    groups = lax.psum(1, "occ")
    local_count = occ_total // groups
    tiles = nvir // 128 if nvir % 128 == 0 else 0
    edge = tiles // EDGE_PART
    if edge >= 1 and tiles - 2 * edge >= 1:
        bounds = [0, edge * 128, nvir - edge * 128, nvir]
    else:
        bounds = [0, nvir]
    chunks = len(bounds) - 1
    ride = step_count == local_count
    rows = integrals.reshape(aux_here, groups, local_count, basis_count)
    rows = jnp.transpose(rows, (1, 0, 2, 3))

    def chunk_product(c):
        return lax.dot_general(
            rows, orbitals[:, bounds[c]:bounds[c + 1]], (((3,), (0,)), ((), ())),
            preferred_element_type=jnp.float32,
        ).astype(jnp.bfloat16)

    first_product = chunk_product(0)
    first_product, late = lax.optimization_barrier((first_product, owner))
    picked = jnp.take(integrals, late, axis=1)
    picked = jnp.dot(
        picked.reshape(aux_here * step_count, basis_count), orbitals,
        preferred_element_type=jnp.float32,
    ).astype(jnp.bfloat16).reshape(aux_here, step_count, nvir)
    pieces = jnp.stack(
        [lax.dynamic_slice_in_dim(picked[:, s, :], vblock[s] * VBLK, VBLK, axis=1) for s in range(step_count)],
        axis=1,
    )

    me = lax.axis_index("occ")
    occ_here = lax.dynamic_slice(occ_energy, (me * local_count,), (local_count,))
    occ_cols = occ_energy[owner]
    vir_blocks = jnp.stack(
        [lax.dynamic_slice(vir_energy, (vblock[s] * VBLK,), (VBLK,)) for s in range(step_count)]
    )
    scale = 1.0 / (aux_here * groups * nvir * VBLK)

    carrier = min(1, chunks - 1) if ride else -1
    if not ride:
        blocks = lax.all_gather(pieces, "occ", axis=0, tiled=True)
    raw = []
    sums = []
    made_at = {}
    pending = []
    for c in range(chunks):
        cols = slice(bounds[c], bounds[c + 1])
        span = bounds[c + 1] - bounds[c]
        product = first_product if c == 0 else chunk_product(c)
        if c == carrier:
            extra = jnp.broadcast_to(pieces[None], (groups, aux_here, step_count, VBLK))
            product = jnp.concatenate([product, extra], axis=3)
        if c >= 1:
            held = (raw[-1],) + tuple(made_at.get(c - 2, ()))
            product, _ = lax.optimization_barrier((product, held))
        got = lax.all_to_all(product, "occ", split_axis=0, concat_axis=0, tiled=True)
        raw.append(got)
        got = got.reshape(groups * aux_here, local_count, got.shape[-1])
        if c == carrier:
            blocks = got[:, :, span:]
            got = got[:, :, :span]
        if c == 0:
            factors = jnp.pad(got, ((0, 0), (0, 0), (0, nvir - span)))
        else:
            factors = lax.dynamic_update_slice(factors, got, (0, 0, bounds[c]))
        if c == carrier:
            whole = raw[-1].reshape(groups * aux_here, local_count, span + VBLK)
            vir_here = jnp.concatenate(
                [vir_energy[cols], jnp.full((VBLK,), jnp.inf, vir_energy.dtype)]
            )
        else:
            whole = lax.optimization_barrier(got)
            vir_here = vir_energy[cols]
        pending.append((whole, vir_here))
        if c >= carrier:
            made = [
                chunk_energies(view, blocks, occ_here, occ_cols, vir_k, vir_blocks, scale)
                for view, vir_k in pending
            ]
            pending = []
            if c < chunks - 1:
                factors, made[0] = lax.optimization_barrier((factors, made[0]))
            made_at[c] = made
            sums.extend(made)
    total = sums[0]
    for extra_sum in sums[1:]:
        total = total + extra_sum
    energies = -total * scale
    return (factors, energies)


def solution(mesh):
    placed = (P(("mol", "occ"), None, None), P("mol", None), P("mol"), P("mol"), P("mol"), P("mol"))
    return jax.shard_map(
        per_device,
        mesh=mesh,
        in_specs=placed,
        out_specs=(P("mol", "occ", None), P(("mol", "occ"), None)),
        check_vma=False,
    )
```

```python
import jax
import jax.numpy as jnp
from jax import lax
from jax.sharding import PartitionSpec as P

VBLK = 192
EDGE_PART = 4


def chunk_energies(factors, blocks, occ_rows, occ_cols, vir_chunk, vir_blocks, scale):
    coulomb = lax.dot_general(
        factors, blocks, (((0,), (0,)), ((), ())), preferred_element_type=jnp.float32
    )
    rows_part = vir_chunk[None, :] - occ_rows[:, None]
    cols_part = vir_blocks - occ_cols[:, None]
    denom = rows_part[:, :, None, None] + cols_part[None, None, :, :]
    return jnp.sum(coulomb * coulomb / denom, axis=(1, 3))


def per_device(integrals, orbitals, occ_energy, vir_energy, owner, vblock):
    aux_here, occ_total, basis_count = integrals.shape
    nvir = orbitals.shape[1]
    step_count = owner.shape[0]
    groups = lax.psum(1, "occ")
    local_count = occ_total // groups
    tiles = nvir // 128 if nvir % 128 == 0 else 0
    edge = tiles // EDGE_PART
    if edge >= 1 and tiles - 2 * edge >= 1:
        bounds = [0, edge * 128, nvir - edge * 128, nvir]
    else:
        bounds = [0, nvir]
    chunks = len(bounds) - 1
    ride = step_count == local_count
    rows = integrals.reshape(aux_here, groups, local_count, basis_count)
    rows = jnp.transpose(rows, (1, 0, 2, 3))

    def chunk_product(c):
        return lax.dot_general(
            rows, orbitals[:, bounds[c]:bounds[c + 1]], (((3,), (0,)), ((), ())),
            preferred_element_type=jnp.float32,
        ).astype(jnp.bfloat16)

    first_product = chunk_product(0)
    first_product, late = lax.optimization_barrier((first_product, owner))
    picked = jnp.take(integrals, late, axis=1)
    picked = jnp.dot(
        picked.reshape(aux_here * step_count, basis_count), orbitals,
        preferred_element_type=jnp.float32,
    ).astype(jnp.bfloat16).reshape(aux_here, step_count, nvir)
    pieces = jnp.stack(
        [lax.dynamic_slice_in_dim(picked[:, s, :], vblock[s] * VBLK, VBLK, axis=1) for s in range(step_count)],
        axis=1,
    )

    me = lax.axis_index("occ")
    occ_here = lax.dynamic_slice(occ_energy, (me * local_count,), (local_count,))
    occ_cols = occ_energy[owner]
    vir_blocks = jnp.stack(
        [lax.dynamic_slice(vir_energy, (vblock[s] * VBLK,), (VBLK,)) for s in range(step_count)]
    )
    scale = 1.0 / (aux_here * groups * nvir * VBLK)

    carrier = min(1, chunks - 1) if ride else -1
    if not ride:
        blocks = lax.all_gather(pieces, "occ", axis=0, tiled=True)
    raw = []
    sums = []
    made_at = {}
    pending = []
    for c in range(chunks):
        cols = slice(bounds[c], bounds[c + 1])
        span = bounds[c + 1] - bounds[c]
        product = first_product if c == 0 else chunk_product(c)
        if c == carrier:
            extra = jnp.broadcast_to(pieces[None], (groups, aux_here, step_count, VBLK))
            product = jnp.concatenate([product, extra], axis=3)
        if c >= 1:
            held = (raw[-1],) + tuple(made_at.get(c - 2, ()))
            product, _ = lax.optimization_barrier((product, held))
        got = lax.all_to_all(product, "occ", split_axis=0, concat_axis=0, tiled=True)
        raw.append(got)
        got = got.reshape(groups * aux_here, local_count, got.shape[-1])
        if c == carrier:
            blocks = got[:, :, span:]
            got = got[:, :, :span]
        if c == 0:
            factors = jnp.pad(got, ((0, 0), (0, 0), (0, nvir - span)))
        else:
            factors = lax.dynamic_update_slice(factors, got, (0, 0, bounds[c]))
        if c == carrier:
            whole = raw[-1].reshape(groups * aux_here, local_count, span + VBLK)
            vir_here = jnp.concatenate(
                [vir_energy[cols], jnp.full((VBLK,), jnp.inf, vir_energy.dtype)]
            )
        else:
            whole = lax.optimization_barrier(got)
            vir_here = vir_energy[cols]
        pending.append((whole, vir_here))
        if c >= carrier:
            made = [
                chunk_energies(view, blocks, occ_here, occ_cols, vir_k, vir_blocks, scale)
                for view, vir_k in pending
            ]
            pending = []
            if c < chunks - 1:
                factors, made[0] = lax.optimization_barrier((factors, made[0]))
            made_at[c] = made
            sums.extend(made)
    total = sums[0]
    for extra_sum in sums[1:]:
        total = total + extra_sum
    energies = -total * scale
    return (factors, energies)


def solution(mesh):
    placed = (P(("mol", "occ"), None, None), P("mol", None), P("mol"), P("mol"), P("mol"), P("mol"))
    return jax.shard_map(
        per_device,
        mesh=mesh,
        in_specs=placed,
        out_specs=(P("mol", "occ", None), P(("mol", "occ"), None)),
        check_vma=False,
    )
```

```python
import jax
import jax.numpy as jnp
from jax import lax
from jax.sharding import PartitionSpec as P

VBLK = 192
EDGE_PART = 4
LEAD_PART = 6


def chunk_energies(factors, blocks, occ_rows, occ_cols, vir_chunk, vir_blocks, scale):
    coulomb = lax.dot_general(
        factors, blocks, (((0,), (0,)), ((), ())), preferred_element_type=jnp.float32
    )
    rows_part = vir_chunk[None, :] - occ_rows[:, None]
    cols_part = vir_blocks - occ_cols[:, None]
    denom = rows_part[:, :, None, None] + cols_part[None, None, :, :]
    return jnp.sum(coulomb * coulomb / denom, axis=(1, 3))


def per_device(integrals, orbitals, occ_energy, vir_energy, owner, vblock):
    aux_here, occ_total, basis_count = integrals.shape
    nvir = orbitals.shape[1]
    step_count = owner.shape[0]
    groups = lax.psum(1, "occ")
    local_count = occ_total // groups
    tiles = nvir // 128 if nvir % 128 == 0 else 0
    edge = tiles // EDGE_PART
    lead = tiles // LEAD_PART
    if edge >= 1 and lead >= 1 and tiles - edge - lead >= 1:
        bounds = [0, lead * 128, nvir - edge * 128, nvir]
    else:
        bounds = [0, nvir]
    chunks = len(bounds) - 1
    ride = step_count == local_count
    rows = integrals.reshape(aux_here, groups, local_count, basis_count)
    rows = jnp.transpose(rows, (1, 0, 2, 3))

    def chunk_product(c):
        return lax.dot_general(
            rows, orbitals[:, bounds[c]:bounds[c + 1]], (((3,), (0,)), ((), ())),
            preferred_element_type=jnp.float32,
        ).astype(jnp.bfloat16)

    first_product = chunk_product(0)
    first_product, late = lax.optimization_barrier((first_product, owner))
    picked = jnp.take(integrals, late, axis=1)
    picked = jnp.dot(
        picked.reshape(aux_here * step_count, basis_count), orbitals,
        preferred_element_type=jnp.float32,
    ).astype(jnp.bfloat16).reshape(aux_here, step_count, nvir)
    pieces = jnp.stack(
        [lax.dynamic_slice_in_dim(picked[:, s, :], vblock[s] * VBLK, VBLK, axis=1) for s in range(step_count)],
        axis=1,
    )

    me = lax.axis_index("occ")
    occ_here = lax.dynamic_slice(occ_energy, (me * local_count,), (local_count,))
    occ_cols = occ_energy[owner]
    vir_blocks = jnp.stack(
        [lax.dynamic_slice(vir_energy, (vblock[s] * VBLK,), (VBLK,)) for s in range(step_count)]
    )
    scale = 1.0 / (aux_here * groups * nvir * VBLK)

    carrier = min(1, chunks - 1) if ride else -1
    if not ride:
        blocks = lax.all_gather(pieces, "occ", axis=0, tiled=True)
    raw = []
    sums = []
    made_at = {}
    pending = []
    for c in range(chunks):
        cols = slice(bounds[c], bounds[c + 1])
        span = bounds[c + 1] - bounds[c]
        product = first_product if c == 0 else chunk_product(c)
        if c == carrier:
            extra = jnp.broadcast_to(pieces[None], (groups, aux_here, step_count, VBLK))
            product = jnp.concatenate([product, extra], axis=3)
        if c >= 1:
            held = (raw[-1],) + tuple(made_at.get(c - 2, ()))
            product, _ = lax.optimization_barrier((product, held))
        got = lax.all_to_all(product, "occ", split_axis=0, concat_axis=0, tiled=True)
        raw.append(got)
        got = got.reshape(groups * aux_here, local_count, got.shape[-1])
        if c == carrier:
            blocks = got[:, :, span:]
            got = got[:, :, :span]
        if c == 0:
            factors = jnp.pad(got, ((0, 0), (0, 0), (0, nvir - span)))
        else:
            factors = lax.dynamic_update_slice(factors, got, (0, 0, bounds[c]))
        if c == carrier:
            whole = raw[-1].reshape(groups * aux_here, local_count, span + VBLK)
            vir_here = jnp.concatenate(
                [vir_energy[cols], jnp.full((VBLK,), jnp.inf, vir_energy.dtype)]
            )
        else:
            whole = lax.optimization_barrier(got)
            vir_here = vir_energy[cols]
        pending.append((whole, vir_here))
        if c >= carrier:
            made = [
                chunk_energies(view, blocks, occ_here, occ_cols, vir_k, vir_blocks, scale)
                for view, vir_k in pending
            ]
            pending = []
            if c < chunks - 1:
                factors, made[0] = lax.optimization_barrier((factors, made[0]))
            made_at[c] = made
            sums.extend(made)
    total = sums[0]
    for extra_sum in sums[1:]:
        total = total + extra_sum
    energies = -total * scale
    return (factors, energies)


def solution(mesh):
    placed = (P(("mol", "occ"), None, None), P("mol", None), P("mol"), P("mol"), P("mol"), P("mol"))
    return jax.shard_map(
        per_device,
        mesh=mesh,
        in_specs=placed,
        out_specs=(P("mol", "occ", None), P(("mol", "occ"), None)),
        check_vma=False,
    )
```

```python
import jax
import jax.numpy as jnp
from jax import lax
from jax.sharding import PartitionSpec as P

VBLK = 192
EDGE_PART = 6
LEAD_PART = 4


def chunk_energies(factors, blocks, occ_rows, occ_cols, vir_chunk, vir_blocks, scale):
    coulomb = lax.dot_general(
        factors, blocks, (((0,), (0,)), ((), ())), preferred_element_type=jnp.float32
    )
    rows_part = vir_chunk[None, :] - occ_rows[:, None]
    cols_part = vir_blocks - occ_cols[:, None]
    denom = rows_part[:, :, None, None] + cols_part[None, None, :, :]
    return jnp.sum(coulomb * coulomb / denom, axis=(1, 3))


def per_device(integrals, orbitals, occ_energy, vir_energy, owner, vblock):
    aux_here, occ_total, basis_count = integrals.shape
    nvir = orbitals.shape[1]
    step_count = owner.shape[0]
    groups = lax.psum(1, "occ")
    local_count = occ_total // groups
    tiles = nvir // 128 if nvir % 128 == 0 else 0
    edge = tiles // EDGE_PART
    lead = tiles // LEAD_PART
    if edge >= 1 and lead >= 1 and tiles - edge - lead >= 1:
        bounds = [0, lead * 128, nvir - edge * 128, nvir]
    else:
        bounds = [0, nvir]
    chunks = len(bounds) - 1
    ride = step_count == local_count
    rows = integrals.reshape(aux_here, groups, local_count, basis_count)
    rows = jnp.transpose(rows, (1, 0, 2, 3))

    def chunk_product(c):
        return lax.dot_general(
            rows, orbitals[:, bounds[c]:bounds[c + 1]], (((3,), (0,)), ((), ())),
            preferred_element_type=jnp.float32,
        ).astype(jnp.bfloat16)

    first_product = chunk_product(0)
    first_product, late = lax.optimization_barrier((first_product, owner))
    picked = jnp.take(integrals, late, axis=1)
    picked = jnp.dot(
        picked.reshape(aux_here * step_count, basis_count), orbitals,
        preferred_element_type=jnp.float32,
    ).astype(jnp.bfloat16).reshape(aux_here, step_count, nvir)
    pieces = jnp.stack(
        [lax.dynamic_slice_in_dim(picked[:, s, :], vblock[s] * VBLK, VBLK, axis=1) for s in range(step_count)],
        axis=1,
    )

    me = lax.axis_index("occ")
    occ_here = lax.dynamic_slice(occ_energy, (me * local_count,), (local_count,))
    occ_cols = occ_energy[owner]
    vir_blocks = jnp.stack(
        [lax.dynamic_slice(vir_energy, (vblock[s] * VBLK,), (VBLK,)) for s in range(step_count)]
    )
    scale = 1.0 / (aux_here * groups * nvir * VBLK)

    carrier = min(1, chunks - 1) if ride else -1
    if not ride:
        blocks = lax.all_gather(pieces, "occ", axis=0, tiled=True)
    raw = []
    sums = []
    made_at = {}
    pending = []
    for c in range(chunks):
        cols = slice(bounds[c], bounds[c + 1])
        span = bounds[c + 1] - bounds[c]
        product = first_product if c == 0 else chunk_product(c)
        if c == carrier:
            extra = jnp.broadcast_to(pieces[None], (groups, aux_here, step_count, VBLK))
            product = jnp.concatenate([product, extra], axis=3)
        if c >= 1:
            held = (raw[-1],) + tuple(made_at.get(c - 2, ()))
            product, _ = lax.optimization_barrier((product, held))
        got = lax.all_to_all(product, "occ", split_axis=0, concat_axis=0, tiled=True)
        raw.append(got)
        got = got.reshape(groups * aux_here, local_count, got.shape[-1])
        if c == carrier:
            blocks = got[:, :, span:]
            got = got[:, :, :span]
        if c == 0:
            factors = jnp.pad(got, ((0, 0), (0, 0), (0, nvir - span)))
        else:
            factors = lax.dynamic_update_slice(factors, got, (0, 0, bounds[c]))
        if c == carrier:
            whole = raw[-1].reshape(groups * aux_here, local_count, span + VBLK)
            vir_here = jnp.concatenate(
                [vir_energy[cols], jnp.full((VBLK,), jnp.inf, vir_energy.dtype)]
            )
        else:
            whole = lax.optimization_barrier(got)
            vir_here = vir_energy[cols]
        pending.append((whole, vir_here))
        if c >= carrier:
            made = [
                chunk_energies(view, blocks, occ_here, occ_cols, vir_k, vir_blocks, scale)
                for view, vir_k in pending
            ]
            pending = []
            if c < chunks - 1:
                factors, made[0] = lax.optimization_barrier((factors, made[0]))
            made_at[c] = made
            sums.extend(made)
    total = sums[0]
    for extra_sum in sums[1:]:
        total = total + extra_sum
    energies = -total * scale
    return (factors, energies)


def solution(mesh):
    placed = (P(("mol", "occ"), None, None), P("mol", None), P("mol"), P("mol"), P("mol"), P("mol"))
    return jax.shard_map(
        per_device,
        mesh=mesh,
        in_specs=placed,
        out_specs=(P("mol", "occ", None), P(("mol", "occ"), None)),
        check_vma=False,
    )
```

```python
import jax
import jax.numpy as jnp
from jax import lax
from jax.sharding import PartitionSpec as P

VBLK = 192
EDGE_PART = 4


def chunk_energies(factors, blocks, occ_rows, occ_cols, vir_chunk, vir_blocks, scale):
    coulomb = lax.dot_general(
        factors, blocks, (((0,), (0,)), ((), ())), preferred_element_type=jnp.float32
    )
    rows_part = vir_chunk[None, :] - occ_rows[:, None]
    cols_part = vir_blocks - occ_cols[:, None]
    denom = rows_part[:, :, None, None] + cols_part[None, None, :, :]
    return jnp.sum(coulomb * coulomb / denom, axis=(1, 3))


def per_device(integrals, orbitals, occ_energy, vir_energy, owner, vblock):
    aux_here, occ_total, basis_count = integrals.shape
    nvir = orbitals.shape[1]
    step_count = owner.shape[0]
    groups = lax.psum(1, "occ")
    local_count = occ_total // groups
    tiles = nvir // 128 if nvir % 128 == 0 else 0
    edge = tiles // EDGE_PART
    if edge >= 1 and tiles - 2 * edge >= 1:
        bounds = [0, edge * 128, nvir - edge * 128, nvir]
    else:
        bounds = [0, nvir]
    chunks = len(bounds) - 1
    ride = step_count == local_count
    rows = integrals.reshape(aux_here, groups, local_count, basis_count)
    rows = jnp.transpose(rows, (1, 0, 2, 3))

    def chunk_product(c):
        return lax.dot_general(
            rows, orbitals[:, bounds[c]:bounds[c + 1]], (((3,), (0,)), ((), ())),
            preferred_element_type=jnp.float32,
        ).astype(jnp.bfloat16)

    first_product = chunk_product(0)
    first_product, late = lax.optimization_barrier((first_product, owner))
    picked = jnp.take(integrals, late, axis=1)
    picked = jnp.dot(
        picked.reshape(aux_here * step_count, basis_count), orbitals,
        preferred_element_type=jnp.float32,
    ).astype(jnp.bfloat16).reshape(aux_here, step_count, nvir)
    pieces = jnp.stack(
        [lax.dynamic_slice_in_dim(picked[:, s, :], vblock[s] * VBLK, VBLK, axis=1) for s in range(step_count)],
        axis=1,
    )

    me = lax.axis_index("occ")
    occ_here = lax.dynamic_slice(occ_energy, (me * local_count,), (local_count,))
    occ_cols = occ_energy[owner]
    vir_blocks = jnp.stack(
        [lax.dynamic_slice(vir_energy, (vblock[s] * VBLK,), (VBLK,)) for s in range(step_count)]
    )
    scale = 1.0 / (aux_here * groups * nvir * VBLK)

    carrier = -1
    wide = -(-VBLK // 128) * 128
    padded = jnp.pad(pieces, ((0, 0), (0, 0), (0, wide - VBLK)))
    blocks = lax.all_gather(padded, "occ", axis=0, tiled=True)[:, :, :VBLK]
    raw = []
    sums = []
    made_at = {}
    pending = []
    for c in range(chunks):
        cols = slice(bounds[c], bounds[c + 1])
        span = bounds[c + 1] - bounds[c]
        product = first_product if c == 0 else chunk_product(c)
        if c == carrier:
            extra = jnp.broadcast_to(pieces[None], (groups, aux_here, step_count, VBLK))
            product = jnp.concatenate([product, extra], axis=3)
        if c >= 1:
            held = (raw[-1],) + tuple(made_at.get(c - 2, ()))
            product, _ = lax.optimization_barrier((product, held))
        got = lax.all_to_all(product, "occ", split_axis=0, concat_axis=0, tiled=True)
        raw.append(got)
        got = got.reshape(groups * aux_here, local_count, got.shape[-1])
        if c == carrier:
            blocks = got[:, :, span:]
            got = got[:, :, :span]
        if c == 0:
            factors = jnp.pad(got, ((0, 0), (0, 0), (0, nvir - span)))
        else:
            factors = lax.dynamic_update_slice(factors, got, (0, 0, bounds[c]))
        if c == carrier:
            whole = raw[-1].reshape(groups * aux_here, local_count, span + VBLK)
            vir_here = jnp.concatenate(
                [vir_energy[cols], jnp.full((VBLK,), jnp.inf, vir_energy.dtype)]
            )
        else:
            whole = lax.optimization_barrier(got)
            vir_here = vir_energy[cols]
        pending.append((whole, vir_here))
        if c >= carrier:
            made = [
                chunk_energies(view, blocks, occ_here, occ_cols, vir_k, vir_blocks, scale)
                for view, vir_k in pending
            ]
            pending = []
            if c < chunks - 1:
                factors, made[0] = lax.optimization_barrier((factors, made[0]))
            made_at[c] = made
            sums.extend(made)
    total = sums[0]
    for extra_sum in sums[1:]:
        total = total + extra_sum
    energies = -total * scale
    return (factors, energies)


def solution(mesh):
    placed = (P(("mol", "occ"), None, None), P("mol", None), P("mol"), P("mol"), P("mol"), P("mol"))
    return jax.shard_map(
        per_device,
        mesh=mesh,
        in_specs=placed,
        out_specs=(P("mol", "occ", None), P(("mol", "occ"), None)),
        check_vma=False,
    )
```

```python
import jax
import jax.numpy as jnp
from jax import lax
from jax.sharding import PartitionSpec as P

VBLK = 192
EDGE_PART = 4
LEAD_PART = 3


def chunk_energies(factors, blocks, occ_rows, occ_cols, vir_chunk, vir_blocks, scale):
    coulomb = lax.dot_general(
        factors, blocks, (((0,), (0,)), ((), ())), preferred_element_type=jnp.float32
    )
    rows_part = vir_chunk[None, :] - occ_rows[:, None]
    cols_part = vir_blocks - occ_cols[:, None]
    denom = rows_part[:, :, None, None] + cols_part[None, None, :, :]
    return jnp.sum(coulomb * coulomb / denom, axis=(1, 3))


def per_device(integrals, orbitals, occ_energy, vir_energy, owner, vblock):
    aux_here, occ_total, basis_count = integrals.shape
    nvir = orbitals.shape[1]
    step_count = owner.shape[0]
    groups = lax.psum(1, "occ")
    local_count = occ_total // groups
    tiles = nvir // 128 if nvir % 128 == 0 else 0
    edge = tiles // EDGE_PART
    lead = tiles // LEAD_PART
    if edge >= 1 and lead >= 1 and tiles - edge - lead >= 1:
        bounds = [0, lead * 128, nvir - edge * 128, nvir]
    else:
        bounds = [0, nvir]
    chunks = len(bounds) - 1
    ride = step_count == local_count
    rows = integrals.reshape(aux_here, groups, local_count, basis_count)
    rows = jnp.transpose(rows, (1, 0, 2, 3))

    def chunk_product(c):
        return lax.dot_general(
            rows, orbitals[:, bounds[c]:bounds[c + 1]], (((3,), (0,)), ((), ())),
            preferred_element_type=jnp.float32,
        ).astype(jnp.bfloat16)

    first_product = chunk_product(0)
    first_product, late = lax.optimization_barrier((first_product, owner))
    picked = jnp.take(integrals, late, axis=1)
    picked = jnp.dot(
        picked.reshape(aux_here * step_count, basis_count), orbitals,
        preferred_element_type=jnp.float32,
    ).astype(jnp.bfloat16).reshape(aux_here, step_count, nvir)
    pieces = jnp.stack(
        [lax.dynamic_slice_in_dim(picked[:, s, :], vblock[s] * VBLK, VBLK, axis=1) for s in range(step_count)],
        axis=1,
    )

    me = lax.axis_index("occ")
    occ_here = lax.dynamic_slice(occ_energy, (me * local_count,), (local_count,))
    occ_cols = occ_energy[owner]
    vir_blocks = jnp.stack(
        [lax.dynamic_slice(vir_energy, (vblock[s] * VBLK,), (VBLK,)) for s in range(step_count)]
    )
    scale = 1.0 / (aux_here * groups * nvir * VBLK)

    carrier = min(1, chunks - 1) if ride else -1
    if not ride:
        blocks = lax.all_gather(pieces, "occ", axis=0, tiled=True)
    raw = []
    sums = []
    made_at = {}
    pending = []
    for c in range(chunks):
        cols = slice(bounds[c], bounds[c + 1])
        span = bounds[c + 1] - bounds[c]
        product = first_product if c == 0 else chunk_product(c)
        if c == carrier:
            extra = jnp.broadcast_to(pieces[None], (groups, aux_here, step_count, VBLK))
            product = jnp.concatenate([product, extra], axis=3)
        if c >= 1:
            held = (raw[-1],) + tuple(made_at.get(c - 2, ()))
            product, _ = lax.optimization_barrier((product, held))
        got = lax.all_to_all(product, "occ", split_axis=0, concat_axis=0, tiled=True)
        raw.append(got)
        got = got.reshape(groups * aux_here, local_count, got.shape[-1])
        if c == carrier:
            blocks = got[:, :, span:]
            got = got[:, :, :span]
        if c == 0:
            factors = jnp.pad(got, ((0, 0), (0, 0), (0, nvir - span)))
        else:
            factors = lax.dynamic_update_slice(factors, got, (0, 0, bounds[c]))
        if c == carrier:
            whole = raw[-1].reshape(groups * aux_here, local_count, span + VBLK)
            vir_here = jnp.concatenate(
                [vir_energy[cols], jnp.full((VBLK,), jnp.inf, vir_energy.dtype)]
            )
        else:
            whole = lax.optimization_barrier(got)
            vir_here = vir_energy[cols]
        pending.append((whole, vir_here))
        if c >= carrier:
            made = [
                chunk_energies(view, blocks, occ_here, occ_cols, vir_k, vir_blocks, scale)
                for view, vir_k in pending
            ]
            pending = []
            if c < chunks - 1:
                factors, made[0] = lax.optimization_barrier((factors, made[0]))
            made_at[c] = made
            sums.extend(made)
    total = sums[0]
    for extra_sum in sums[1:]:
        total = total + extra_sum
    energies = -total * scale
    return (factors, energies)


def solution(mesh):
    placed = (P(("mol", "occ"), None, None), P("mol", None), P("mol"), P("mol"), P("mol"), P("mol"))
    return jax.shard_map(
        per_device,
        mesh=mesh,
        in_specs=placed,
        out_specs=(P("mol", "occ", None), P(("mol", "occ"), None)),
        check_vma=False,
    )
```

```python
import jax
import jax.numpy as jnp
from jax import lax
from jax.sharding import PartitionSpec as P

VBLK = 192
EDGE_PART = 4


def chunk_energies(factors, blocks, occ_rows, occ_cols, vir_chunk, vir_blocks, scale):
    coulomb = lax.dot_general(
        factors, blocks, (((0,), (0,)), ((), ())), preferred_element_type=jnp.float32
    )
    rows_part = vir_chunk[None, :] - occ_rows[:, None]
    cols_part = vir_blocks - occ_cols[:, None]
    denom = rows_part[:, :, None, None] + cols_part[None, None, :, :]
    return jnp.sum(coulomb * coulomb / denom, axis=(1, 3))


def per_device(integrals, orbitals, occ_energy, vir_energy, owner, vblock):
    aux_here, occ_total, basis_count = integrals.shape
    nvir = orbitals.shape[1]
    step_count = owner.shape[0]
    groups = lax.psum(1, "occ")
    local_count = occ_total // groups
    tiles = nvir // 128 if nvir % 128 == 0 else 0
    edge = tiles // EDGE_PART
    if edge >= 1 and tiles - 2 * edge >= 1:
        bounds = [0, edge * 128, nvir - edge * 128, nvir]
    else:
        bounds = [0, nvir]
    chunks = len(bounds) - 1
    ride = step_count == local_count
    rows = integrals.reshape(aux_here, groups, local_count, basis_count)
    rows = jnp.transpose(rows, (1, 0, 2, 3))

    def chunk_product(c):
        return lax.dot_general(
            rows, orbitals[:, bounds[c]:bounds[c + 1]], (((3,), (0,)), ((), ())),
            preferred_element_type=jnp.float32,
        ).astype(jnp.bfloat16)

    first_product = chunk_product(0)
    first_product, late = lax.optimization_barrier((first_product, owner))
    picked = jnp.take(integrals, late, axis=1)
    picked = jnp.dot(
        picked.reshape(aux_here * step_count, basis_count), orbitals,
        preferred_element_type=jnp.float32,
    ).astype(jnp.bfloat16).reshape(aux_here, step_count, nvir)
    pieces = jnp.stack(
        [lax.dynamic_slice_in_dim(picked[:, s, :], vblock[s] * VBLK, VBLK, axis=1) for s in range(step_count)],
        axis=1,
    )

    me = lax.axis_index("occ")
    occ_here = lax.dynamic_slice(occ_energy, (me * local_count,), (local_count,))
    occ_cols = occ_energy[owner]
    vir_blocks = jnp.stack(
        [lax.dynamic_slice(vir_energy, (vblock[s] * VBLK,), (VBLK,)) for s in range(step_count)]
    )
    scale = 1.0 / (aux_here * groups * nvir * VBLK)

    carrier = -1
    if groups <= 16:
        got_pieces = [pieces]
        for shift in range(1, groups):
            pairs = [(d, (d - shift) % groups) for d in range(groups)]
            got_pieces.append(lax.ppermute(pieces, "occ", pairs))
        stacked = jnp.stack(got_pieces)
        blocks = jnp.roll(stacked, me, axis=0).reshape(groups * aux_here, step_count, VBLK)
    else:
        blocks = lax.all_gather(pieces, "occ", axis=0, tiled=True)
    raw = []
    sums = []
    made_at = {}
    pending = []
    for c in range(chunks):
        cols = slice(bounds[c], bounds[c + 1])
        span = bounds[c + 1] - bounds[c]
        product = first_product if c == 0 else chunk_product(c)
        if c == carrier:
            extra = jnp.broadcast_to(pieces[None], (groups, aux_here, step_count, VBLK))
            product = jnp.concatenate([product, extra], axis=3)
        if c >= 1:
            held = (raw[-1],) + tuple(made_at.get(c - 2, ()))
            product, _ = lax.optimization_barrier((product, held))
        got = lax.all_to_all(product, "occ", split_axis=0, concat_axis=0, tiled=True)
        raw.append(got)
        got = got.reshape(groups * aux_here, local_count, got.shape[-1])
        if c == carrier:
            blocks = got[:, :, span:]
            got = got[:, :, :span]
        if c == 0:
            factors = jnp.pad(got, ((0, 0), (0, 0), (0, nvir - span)))
        else:
            factors = lax.dynamic_update_slice(factors, got, (0, 0, bounds[c]))
        if c == carrier:
            whole = raw[-1].reshape(groups * aux_here, local_count, span + VBLK)
            vir_here = jnp.concatenate(
                [vir_energy[cols], jnp.full((VBLK,), jnp.inf, vir_energy.dtype)]
            )
        else:
            whole = lax.optimization_barrier(got)
            vir_here = vir_energy[cols]
        pending.append((whole, vir_here))
        if c >= carrier:
            made = [
                chunk_energies(view, blocks, occ_here, occ_cols, vir_k, vir_blocks, scale)
                for view, vir_k in pending
            ]
            pending = []
            if c < chunks - 1:
                factors, made[0] = lax.optimization_barrier((factors, made[0]))
            made_at[c] = made
            sums.extend(made)
    total = sums[0]
    for extra_sum in sums[1:]:
        total = total + extra_sum
    energies = -total * scale
    return (factors, energies)


def solution(mesh):
    placed = (P(("mol", "occ"), None, None), P("mol", None), P("mol"), P("mol"), P("mol"), P("mol"))
    return jax.shard_map(
        per_device,
        mesh=mesh,
        in_specs=placed,
        out_specs=(P("mol", "occ", None), P(("mol", "occ"), None)),
        check_vma=False,
    )
```

```python
import jax
import jax.numpy as jnp
from jax import lax
from jax.sharding import PartitionSpec as P

VBLK = 192
EDGE_PART = 4
LEAD_PART = 12


def chunk_energies(factors, blocks, occ_rows, occ_cols, vir_chunk, vir_blocks, scale):
    coulomb = lax.dot_general(
        factors, blocks, (((0,), (0,)), ((), ())), preferred_element_type=jnp.float32
    )
    rows_part = vir_chunk[None, :] - occ_rows[:, None]
    cols_part = vir_blocks - occ_cols[:, None]
    denom = rows_part[:, :, None, None] + cols_part[None, None, :, :]
    return jnp.sum(coulomb * coulomb / denom, axis=(1, 3))


def per_device(integrals, orbitals, occ_energy, vir_energy, owner, vblock):
    aux_here, occ_total, basis_count = integrals.shape
    nvir = orbitals.shape[1]
    step_count = owner.shape[0]
    groups = lax.psum(1, "occ")
    local_count = occ_total // groups
    tiles = nvir // 128 if nvir % 128 == 0 else 0
    edge = tiles // EDGE_PART
    lead = tiles // LEAD_PART
    if edge >= 1 and lead >= 1 and tiles - edge - lead >= 1:
        bounds = [0, lead * 128, nvir - edge * 128, nvir]
    else:
        bounds = [0, nvir]
    chunks = len(bounds) - 1
    ride = step_count == local_count
    rows = integrals.reshape(aux_here, groups, local_count, basis_count)
    rows = jnp.transpose(rows, (1, 0, 2, 3))

    def chunk_product(c):
        return lax.dot_general(
            rows, orbitals[:, bounds[c]:bounds[c + 1]], (((3,), (0,)), ((), ())),
            preferred_element_type=jnp.float32,
        ).astype(jnp.bfloat16)

    first_product = chunk_product(0)
    first_product, late = lax.optimization_barrier((first_product, owner))
    picked = jnp.take(integrals, late, axis=1)
    picked = jnp.dot(
        picked.reshape(aux_here * step_count, basis_count), orbitals,
        preferred_element_type=jnp.float32,
    ).astype(jnp.bfloat16).reshape(aux_here, step_count, nvir)
    pieces = jnp.stack(
        [lax.dynamic_slice_in_dim(picked[:, s, :], vblock[s] * VBLK, VBLK, axis=1) for s in range(step_count)],
        axis=1,
    )

    me = lax.axis_index("occ")
    occ_here = lax.dynamic_slice(occ_energy, (me * local_count,), (local_count,))
    occ_cols = occ_energy[owner]
    vir_blocks = jnp.stack(
        [lax.dynamic_slice(vir_energy, (vblock[s] * VBLK,), (VBLK,)) for s in range(step_count)]
    )
    scale = 1.0 / (aux_here * groups * nvir * VBLK)

    carrier = min(1, chunks - 1) if ride else -1
    if not ride:
        blocks = lax.all_gather(pieces, "occ", axis=0, tiled=True)
    raw = []
    sums = []
    made_at = {}
    pending = []
    for c in range(chunks):
        cols = slice(bounds[c], bounds[c + 1])
        span = bounds[c + 1] - bounds[c]
        product = first_product if c == 0 else chunk_product(c)
        if c == carrier:
            extra = jnp.broadcast_to(pieces[None], (groups, aux_here, step_count, VBLK))
            product = jnp.concatenate([product, extra], axis=3)
        if c >= 1:
            held = (raw[-1],) + tuple(made_at.get(c - 2, ()))
            product, _ = lax.optimization_barrier((product, held))
        got = lax.all_to_all(product, "occ", split_axis=0, concat_axis=0, tiled=True)
        raw.append(got)
        got = got.reshape(groups * aux_here, local_count, got.shape[-1])
        if c == carrier:
            blocks = got[:, :, span:]
            got = got[:, :, :span]
        if c == 0:
            factors = jnp.pad(got, ((0, 0), (0, 0), (0, nvir - span)))
        else:
            factors = lax.dynamic_update_slice(factors, got, (0, 0, bounds[c]))
        if c == carrier:
            whole = raw[-1].reshape(groups * aux_here, local_count, span + VBLK)
            vir_here = jnp.concatenate(
                [vir_energy[cols], jnp.full((VBLK,), jnp.inf, vir_energy.dtype)]
            )
        else:
            whole = lax.optimization_barrier(got)
            vir_here = vir_energy[cols]
        pending.append((whole, vir_here))
        if c >= carrier:
            made = [
                chunk_energies(view, blocks, occ_here, occ_cols, vir_k, vir_blocks, scale)
                for view, vir_k in pending
            ]
            pending = []
            if c < chunks - 1:
                factors, made[0] = lax.optimization_barrier((factors, made[0]))
            made_at[c] = made
            sums.extend(made)
    total = sums[0]
    for extra_sum in sums[1:]:
        total = total + extra_sum
    energies = -total * scale
    return (factors, energies)


def solution(mesh):
    placed = (P(("mol", "occ"), None, None), P("mol", None), P("mol"), P("mol"), P("mol"), P("mol"))
    return jax.shard_map(
        per_device,
        mesh=mesh,
        in_specs=placed,
        out_specs=(P("mol", "occ", None), P(("mol", "occ"), None)),
        check_vma=False,
    )
```
